768 devices in a mesh: occ: 16 (over y, core), virt: 12 (over z), rep: 4 (over x).
Axes of the slice: x: 4, y: 8, z: 12, core: 2. Of those that a mesh axis runs over, the one named last changes fastest.
Arguments:
- amplitudes: bfloat16 [4096, 15360], P(('occ', 'rep'), 'virt'), may hold values from -6 to 6
- integrals: bfloat16 [15360, 3072], P(('occ', 'rep'), 'virt'), may hold values from -0.125 to 0.125
- cd_irrep: int32 [15360], P(('occ', 'rep')), may hold values from 0 to 7
- ab_irrep: int32 [3072], P('virt'), may hold values from 0 to 7
Outputs:
- residual: float32 [4096, 3072], P(('occ', 'rep'), 'virt')
The draws below stay inside these ranges and needn't reach their ends.
Inputs may be any that keep to these rules, and one draw needn't show every extreme that they name: `cd_irrep`: irreps of the eight D2h irreducible representations. `ab_irrep`: irreps of the eight D2h irreducible representations.
All inputs are finite; a program needn't handle non-finite values.
Results may differ from the reference program's by a relative error of at most 0.0003.
Values may be sent and summed in bfloat16 or wider, within the bound.
No kernel may reach another device: no remote copies, remote signals or barrier semaphores. Data moves between devices by JAX's collectives and lax.ppermute only.
A program may use at most 32 MiB of HBM per device.

```python
import jax
import jax.numpy as jnp

OPAIR = 4096
CD = 15360
AB = 3072


def touch_ends(drawn, own_key, least, high):
    longest = drawn.shape.index(max(drawn.shape))
    spots = []
    for shift in (0, 1):
        where = [jax.random.randint(jax.random.fold_in(own_key, axis), (), 0, length) for axis, length in enumerate(drawn.shape)]
        where[longest] = (where[longest] + shift) % drawn.shape[longest]
        spots.append(tuple(where))
    return drawn.at[spots[0]].set(least).at[spots[1]].set(high)


def shard_levels(rng, shape, pieces, smallest, largest):
    level = 1.0
    for dim, blocks in pieces:
        draws = jax.random.uniform(jax.random.fold_in(jax.random.fold_in(rng, 6), dim), (blocks,), jnp.float32, smallest / len(pieces), largest / len(pieces))
        level = level * jnp.repeat(jnp.exp(draws), shape[dim] // blocks).reshape((-1,) + (1,) * (len(shape) - 1 - dim))
    return level


def noise(own_key, extent, deviation, most, pieces=(), kind=jnp.bfloat16):
    drawn = jax.random.normal(own_key, extent, jnp.float32) * deviation
    if len(pieces) > 0:
        drawn = shard_levels(own_key, extent, pieces, -0.22, 0.18) * drawn
    return jnp.clip(drawn, min=-most, max=most).astype(kind)


def setup_inputs(seed: int = 0) -> dict:
    key_list = jax.random.split(jax.random.key(seed), 5)
    return {
        "amplitudes": noise(key_list[0], (OPAIR, CD), 1.0, 6.0, ((0, 64), (1, 12))),
        "integrals": noise(key_list[1], (CD, AB), (CD // 8) ** -0.5, 0.125, ((0, 64), (1, 12))),
        "cd_irrep": touch_ends(jax.random.randint(key_list[2], (CD,), 0, 8), jax.random.fold_in(key_list[2], 1), 0, 7).astype(jnp.int32),
        "ab_irrep": touch_ends(jax.random.randint(key_list[3], (AB,), 0, 8), jax.random.fold_in(key_list[3], 1), 0, 7).astype(jnp.int32),
    }


def reference(amplitudes, integrals, cd_irrep, ab_irrep):
    allowed = cd_irrep[:, None] == ab_irrep[None, :]
    masked = jnp.where(allowed, integrals, jnp.zeros_like(integrals))
    return jnp.dot(amplitudes, masked, preferred_element_type=jnp.float32)
```

```python
import math

import jax
import jax.numpy as jnp
from jax import lax
from jax.sharding import PartitionSpec as P


def local(amplitudes, integrals, cd_irrep, ab_irrep, n_rep):
    rows, cols = amplitudes.shape
    kb, nb = integrals.shape
    atom = math.gcd(cols, kb)
    per_v = cols // atom
    per_k = kb // atom
    assert per_v % n_rep == 0 and per_k <= n_rep
    r = lax.axis_index("rep")

    masked = jnp.where(cd_irrep[:, None] == ab_irrep[None, :], integrals, jnp.zeros_like(integrals))

    a = amplitudes.reshape(rows, per_v // n_rep, n_rep, atom)
    a = lax.all_to_all(a, "rep", split_axis=2, concat_axis=0, tiled=True)
    a = a.reshape(n_rep * rows, (per_v // n_rep) * atom)
    a = lax.all_gather(a, "virt", axis=1, tiled=True)

    b = masked.reshape(per_k, atom, nb)
    b = jnp.concatenate([b, jnp.zeros((n_rep - per_k, atom, nb), b.dtype)], axis=0)
    dest = jnp.arange(n_rep)
    send_idx = (dest - per_k * r) % n_rep
    b = jnp.take(b, send_idx, axis=0)
    b = lax.all_to_all(b, "rep", split_axis=0, concat_axis=0, tiled=True)
    got = (r - per_k * dest) % n_rep
    keep = jnp.nonzero(got < per_k, size=per_k)[0]
    b = jnp.take(b, keep, axis=0)
    b = lax.all_gather(b, "occ", axis=0, tiled=True)
    b = b.reshape(-1, nb)

    partial_sum = jnp.dot(a, b, preferred_element_type=jnp.float32)
    return lax.psum_scatter(partial_sum, "rep", scatter_dimension=0, tiled=True)


def solution(mesh):
    n_rep = mesh.shape["rep"]
    in_specs = (P(("occ", "rep"), "virt"), P(("occ", "rep"), "virt"), P(("occ", "rep")), P("virt"))
    out_specs = P(("occ", "rep"), "virt")

    def body(amplitudes, integrals, cd_irrep, ab_irrep):
        return local(amplitudes, integrals, cd_irrep, ab_irrep, n_rep)

    return jax.shard_map(body, mesh=mesh, in_specs=in_specs, out_specs=out_specs, check_vma=False)
```

```python
import math

import jax
import jax.numpy as jnp
from jax import lax
from jax.sharding import PartitionSpec as P


def local(amplitudes, integrals, cd_irrep, ab_irrep, n_rep):
    rows, cols = amplitudes.shape
    kb, nb = integrals.shape
    atom = math.gcd(cols, kb)
    per_v = cols // atom
    per_k = kb // atom
    assert per_v % n_rep == 0 and per_k <= n_rep
    r = lax.axis_index("rep")

    masked = jnp.where(cd_irrep[:, None] == ab_irrep[None, :], integrals, jnp.zeros_like(integrals))

    a = amplitudes.reshape(rows, per_v // n_rep, n_rep, atom)
    a = lax.all_to_all(a, "rep", split_axis=2, concat_axis=0, tiled=True)
    a = a.reshape(n_rep * rows, (per_v // n_rep) * atom)
    a = lax.all_gather(a, "virt", axis=1, tiled=True)

    b = masked.reshape(per_k, atom, nb)
    b = jnp.concatenate([b, jnp.zeros((n_rep - per_k, atom, nb), b.dtype)], axis=0)
    dest = jnp.arange(n_rep)
    send_idx = (dest - per_k * r) % n_rep
    b = jnp.take(b, send_idx, axis=0)
    b = lax.all_to_all(b, "rep", split_axis=0, concat_axis=0, tiled=True)
    got = (r - per_k * dest) % n_rep
    keep = jnp.nonzero(got < per_k, size=per_k)[0]
    b = jnp.take(b, keep, axis=0)
    n_occ = lax.axis_size("occ")
    b = jnp.broadcast_to(b[None], (n_occ,) + b.shape)
    b = lax.all_to_all(b, "occ", split_axis=0, concat_axis=0, tiled=True)
    b = b.reshape(-1, nb)

    partial_sum = jnp.dot(a, b, preferred_element_type=jnp.float32)
    partial_sum = partial_sum.reshape(n_rep, rows, nb)
    partial_sum = lax.all_to_all(partial_sum, "rep", split_axis=0, concat_axis=0, tiled=True)
    return jnp.sum(partial_sum, axis=0)


def solution(mesh):
    n_rep = mesh.shape["rep"]
    in_specs = (P(("occ", "rep"), "virt"), P(("occ", "rep"), "virt"), P(("occ", "rep")), P("virt"))
    out_specs = P(("occ", "rep"), "virt")

    def body(amplitudes, integrals, cd_irrep, ab_irrep):
        return local(amplitudes, integrals, cd_irrep, ab_irrep, n_rep)

    return jax.shard_map(body, mesh=mesh, in_specs=in_specs, out_specs=out_specs, check_vma=False)
```

```python
import math

import jax
import jax.numpy as jnp
from jax import lax
from jax.sharding import Mesh
from jax.sharding import PartitionSpec as P


def local(amplitudes, integrals, cd_irrep, ab_irrep, n_rep, n_oy, n_oc):
    rows, cols = amplitudes.shape
    kb, nb = integrals.shape
    atom = math.gcd(cols, kb)
    per_v = cols // atom
    per_k = kb // atom
    assert per_v % n_rep == 0 and per_k == n_rep - 1
    r = lax.axis_index("rep")

    a = amplitudes.reshape(rows, per_v // n_rep, n_rep, atom)
    a = jnp.transpose(a, (2, 0, 1, 3)).reshape(n_rep, rows, (per_v // n_rep) * atom)
    a = lax.all_to_all(a, "rep", split_axis=0, concat_axis=0, tiled=True)
    a = a.reshape(n_rep * rows, (per_v // n_rep) * atom)
    a, integrals, cd_irrep, ab_irrep = lax.optimization_barrier((a, integrals, cd_irrep, ab_irrep))
    a = lax.all_gather(a, "virt", axis=1, tiled=True)

    masked = jnp.where(cd_irrep[:, None] == ab_irrep[None, :], integrals, jnp.zeros_like(integrals))
    b = masked.reshape(per_k, atom, nb)
    b = jnp.concatenate([b, jnp.zeros((n_rep - per_k, atom, nb), b.dtype)], axis=0)
    b = lax.dynamic_slice_in_dim(jnp.concatenate([b, b], axis=0), r, n_rep, axis=0)
    b = lax.all_to_all(b, "rep", split_axis=0, concat_axis=0, tiled=True)
    q = (n_rep - 1 - r) % n_rep
    skip = (jnp.arange(per_k) >= q)[:, None, None]
    b = jnp.where(skip, b[1:], b[:-1])
    b = jnp.broadcast_to(b[None], (n_oy,) + b.shape)
    b = lax.all_to_all(b, "oy", split_axis=0, concat_axis=0, tiled=True)
    b = jnp.broadcast_to(b[None], (n_oc,) + b.shape)
    b = lax.all_to_all(b, "oc", split_axis=0, concat_axis=0, tiled=True)
    b = jnp.moveaxis(b, 0, 1).reshape(-1, nb)

    partial_sum = jnp.dot(a, b, preferred_element_type=jnp.float32)
    partial_sum = partial_sum.reshape(n_rep, rows, nb)
    partial_sum = lax.all_to_all(partial_sum, "rep", split_axis=0, concat_axis=0, tiled=True)
    return jnp.sum(partial_sum, axis=0)


def solution(mesh):
    n_occ, n_virt, n_rep = mesh.shape["occ"], mesh.shape["virt"], mesh.shape["rep"]
    n_oc = 2 if n_occ % 2 == 0 else 1
    n_oy = n_occ // n_oc
    fine = Mesh(mesh.devices.reshape(n_oy, n_oc, n_virt, n_rep), ("oy", "oc", "virt", "rep"))
    rows_spec = ("oy", "oc", "rep")
    in_specs = (P(rows_spec, "virt"), P(rows_spec, "virt"), P(rows_spec), P("virt"))
    out_specs = P(rows_spec, "virt")

    def body(amplitudes, integrals, cd_irrep, ab_irrep):
        return local(amplitudes, integrals, cd_irrep, ab_irrep, n_rep, n_oy, n_oc)

    return jax.shard_map(body, mesh=fine, in_specs=in_specs, out_specs=out_specs, check_vma=False)
```

```python
import math

import jax
import jax.numpy as jnp
from jax import lax
from jax.sharding import Mesh
from jax.sharding import PartitionSpec as P


def local(amplitudes, integrals, cd_irrep, ab_irrep, n_rep, n_oy, n_oc):
    rows, cols = amplitudes.shape
    kb, nb = integrals.shape
    atom = math.gcd(cols, kb)
    per_v = cols // atom
    per_k = kb // atom
    assert per_v % n_rep == 0 and per_k == n_rep - 1
    r = lax.axis_index("rep")

    a = amplitudes.reshape(rows, per_v // n_rep, n_rep, atom)
    a = jnp.transpose(a, (2, 0, 1, 3)).reshape(n_rep, rows, (per_v // n_rep) * atom)
    a = lax.all_to_all(a, "rep", split_axis=0, concat_axis=0, tiled=True)
    a = a.reshape(n_rep * rows, (per_v // n_rep) * atom)
    a, integrals, cd_irrep, ab_irrep = lax.optimization_barrier((a, integrals, cd_irrep, ab_irrep))
    a = lax.all_gather(a, "virt", axis=0, tiled=False)

    masked = jnp.where(cd_irrep[:, None] == ab_irrep[None, :], integrals, jnp.zeros_like(integrals))
    b = masked.reshape(per_k, atom, nb)
    b = jnp.concatenate([b, jnp.zeros((n_rep - per_k, atom, nb), b.dtype)], axis=0)
    b = lax.dynamic_slice_in_dim(jnp.concatenate([b, b], axis=0), r, n_rep, axis=0)
    b = lax.all_to_all(b, "rep", split_axis=0, concat_axis=0, tiled=True)
    q = (n_rep - 1 - r) % n_rep
    skip = (jnp.arange(per_k) >= q)[:, None, None]
    b = jnp.where(skip, b[1:], b[:-1])
    b = jnp.broadcast_to(b[None], (n_oy,) + b.shape)
    b = lax.all_to_all(b, "oy", split_axis=0, concat_axis=0, tiled=True)
    b = jnp.broadcast_to(b[None], (n_oc,) + b.shape)
    b = lax.all_to_all(b, "oc", split_axis=0, concat_axis=0, tiled=True)
    b = jnp.moveaxis(b, 0, 1).reshape(a.shape[0], a.shape[2], nb)

    partial_sum = jnp.einsum("vmc,vcn->mn", a, b, preferred_element_type=jnp.float32)
    partial_sum = partial_sum.reshape(n_rep, rows, nb)
    partial_sum = lax.all_to_all(partial_sum, "rep", split_axis=0, concat_axis=0, tiled=True)
    return jnp.sum(partial_sum, axis=0)


def solution(mesh):
    n_occ, n_virt, n_rep = mesh.shape["occ"], mesh.shape["virt"], mesh.shape["rep"]
    n_oc = 2 if n_occ % 2 == 0 else 1
    n_oy = n_occ // n_oc
    fine = Mesh(mesh.devices.reshape(n_oy, n_oc, n_virt, n_rep), ("oy", "oc", "virt", "rep"))
    rows_spec = ("oy", "oc", "rep")
    in_specs = (P(rows_spec, "virt"), P(rows_spec, "virt"), P(rows_spec), P("virt"))
    out_specs = P(rows_spec, "virt")

    def body(amplitudes, integrals, cd_irrep, ab_irrep):
        return local(amplitudes, integrals, cd_irrep, ab_irrep, n_rep, n_oy, n_oc)

    return jax.shard_map(body, mesh=fine, in_specs=in_specs, out_specs=out_specs, check_vma=False)
```

```python
import math

import jax
import jax.numpy as jnp
from jax import lax
from jax.sharding import Mesh
from jax.sharding import PartitionSpec as P


def local(amplitudes, integrals, cd_irrep, ab_irrep, n_rep, n_oy, n_oc):
    rows, cols = amplitudes.shape
    kb, nb = integrals.shape
    atom = math.gcd(cols, kb)
    per_v = cols // atom
    per_k = kb // atom
    assert per_v % n_rep == 0 and per_k == n_rep - 1
    r = lax.axis_index("rep")

    a = amplitudes.reshape(rows, per_v // n_rep, n_rep, atom)
    a = jnp.transpose(a, (2, 0, 1, 3)).reshape(n_rep, rows, (per_v // n_rep) * atom)
    a = lax.all_to_all(a, "rep", split_axis=0, concat_axis=0, tiled=True)
    a = a.reshape(n_rep * rows, (per_v // n_rep) * atom)
    a, integrals, cd_irrep, ab_irrep = lax.optimization_barrier((a, integrals, cd_irrep, ab_irrep))
    h = a.shape[0] // 2
    a1 = lax.all_gather(a[:h], "virt", axis=0, tiled=False)
    a1, a_rest = lax.optimization_barrier((a1, a[h:]))
    a2 = lax.all_gather(a_rest, "virt", axis=0, tiled=False)

    masked = jnp.where(cd_irrep[:, None] == ab_irrep[None, :], integrals, jnp.zeros_like(integrals))
    b = masked.reshape(per_k, atom, nb)
    b = jnp.concatenate([b, jnp.zeros((n_rep - per_k, atom, nb), b.dtype)], axis=0)
    b = lax.dynamic_slice_in_dim(jnp.concatenate([b, b], axis=0), r, n_rep, axis=0)
    b = lax.all_to_all(b, "rep", split_axis=0, concat_axis=0, tiled=True)
    q = (n_rep - 1 - r) % n_rep
    skip = (jnp.arange(per_k) >= q)[:, None, None]
    b = jnp.where(skip, b[1:], b[:-1])
    b = jnp.broadcast_to(b[None], (n_oy,) + b.shape)
    b = lax.all_to_all(b, "oy", split_axis=0, concat_axis=0, tiled=True)
    b = jnp.broadcast_to(b[None], (n_oc,) + b.shape)
    b = lax.all_to_all(b, "oc", split_axis=0, concat_axis=0, tiled=True)
    b = jnp.moveaxis(b, 0, 1).reshape(a1.shape[0], a1.shape[2], nb)

    partial_sum = jnp.concatenate([
        jnp.einsum("vmc,vcn->mn", a1, b, preferred_element_type=jnp.float32),
        jnp.einsum("vmc,vcn->mn", a2, b, preferred_element_type=jnp.float32)], axis=0)
    partial_sum = partial_sum.reshape(n_rep, rows, nb)
    partial_sum = lax.all_to_all(partial_sum, "rep", split_axis=0, concat_axis=0, tiled=True)
    return jnp.sum(partial_sum, axis=0)


def solution(mesh):
    n_occ, n_virt, n_rep = mesh.shape["occ"], mesh.shape["virt"], mesh.shape["rep"]
    n_oc = 2 if n_occ % 2 == 0 else 1
    n_oy = n_occ // n_oc
    fine = Mesh(mesh.devices.reshape(n_oy, n_oc, n_virt, n_rep), ("oy", "oc", "virt", "rep"))
    rows_spec = ("oy", "oc", "rep")
    in_specs = (P(rows_spec, "virt"), P(rows_spec, "virt"), P(rows_spec), P("virt"))
    out_specs = P(rows_spec, "virt")

    def body(amplitudes, integrals, cd_irrep, ab_irrep):
        return local(amplitudes, integrals, cd_irrep, ab_irrep, n_rep, n_oy, n_oc)

    return jax.shard_map(body, mesh=fine, in_specs=in_specs, out_specs=out_specs, check_vma=False)
```

```python
import math

import jax
import jax.numpy as jnp
from jax import lax
from jax.sharding import Mesh
from jax.sharding import PartitionSpec as P


def local(amplitudes, integrals, cd_irrep, ab_irrep, n_rep, n_oy, n_oc):
    rows, cols = amplitudes.shape
    kb, nb = integrals.shape
    atom = math.gcd(cols, kb)
    per_v = cols // atom
    per_k = kb // atom
    assert per_v % n_rep == 0 and per_k == n_rep - 1
    r = lax.axis_index("rep")

    a = amplitudes.reshape(rows, per_v // n_rep, n_rep, atom)
    a = jnp.transpose(a, (2, 0, 1, 3)).reshape(n_rep, rows, (per_v // n_rep) * atom)
    a = lax.all_to_all(a, "rep", split_axis=0, concat_axis=0, tiled=True)
    a = a.reshape(n_rep * rows, (per_v // n_rep) * atom)
    a, integrals, cd_irrep, ab_irrep = lax.optimization_barrier((a, integrals, cd_irrep, ab_irrep))
    a = lax.all_gather(a, "virt", axis=0, tiled=False)

    masked = jnp.where(cd_irrep[:, None] == ab_irrep[None, :], integrals, jnp.zeros_like(integrals))
    b = masked.reshape(per_k, atom, nb)
    b = jnp.concatenate([b, jnp.zeros((n_rep - per_k, atom, nb), b.dtype)], axis=0)
    b = lax.dynamic_slice_in_dim(jnp.concatenate([b, b], axis=0), r, n_rep, axis=0)
    b = lax.all_to_all(b, "rep", split_axis=0, concat_axis=0, tiled=True)
    q = (n_rep - 1 - r) % n_rep
    skip = (jnp.arange(per_k) >= q)[:, None, None]
    b = jnp.where(skip, b[1:], b[:-1])
    b = jnp.broadcast_to(b[None], (n_oy,) + b.shape)
    b = lax.all_to_all(b, "oy", split_axis=0, concat_axis=0, tiled=True)
    b = jnp.broadcast_to(b[None], (n_oc,) + b.shape)
    b = lax.all_to_all(b, "oc", split_axis=0, concat_axis=0, tiled=True)
    b = jnp.moveaxis(b, 0, 1).reshape(a.shape[0], a.shape[2], nb)

    a = a.reshape(a.shape[0], n_rep, rows, a.shape[2])
    def part(g):
        rows_g = lax.dynamic_index_in_dim(a, g, axis=1, keepdims=False)
        return jnp.einsum("vmc,vcn->mn", rows_g, b, preferred_element_type=jnp.float32)
    total = None
    for s in range(1, n_rep):
        sent = lax.ppermute(part((r + s) % n_rep), "rep", [(j, (j + s) % n_rep) for j in range(n_rep)])
        total = sent if total is None else total + sent
    return total + part(r)


def solution(mesh):
    n_occ, n_virt, n_rep = mesh.shape["occ"], mesh.shape["virt"], mesh.shape["rep"]
    n_oc = 2 if n_occ % 2 == 0 else 1
    n_oy = n_occ // n_oc
    fine = Mesh(mesh.devices.reshape(n_oy, n_oc, n_virt, n_rep), ("oy", "oc", "virt", "rep"))
    rows_spec = ("oy", "oc", "rep")
    in_specs = (P(rows_spec, "virt"), P(rows_spec, "virt"), P(rows_spec), P("virt"))
    out_specs = P(rows_spec, "virt")

    def body(amplitudes, integrals, cd_irrep, ab_irrep):
        return local(amplitudes, integrals, cd_irrep, ab_irrep, n_rep, n_oy, n_oc)

    return jax.shard_map(body, mesh=fine, in_specs=in_specs, out_specs=out_specs, check_vma=False)
```

```python
import math

import jax
import jax.numpy as jnp
from jax import lax
from jax.sharding import Mesh
from jax.sharding import PartitionSpec as P


def local(amplitudes, integrals, cd_irrep, ab_irrep, n_rep, n_virt, n_oy, n_oc):
    rows, cols = amplitudes.shape
    kb, nb = integrals.shape
    atom = math.gcd(cols, kb)
    per_v = cols // atom
    per_k = kb // atom
    assert per_v % n_rep == 0 and per_k == n_rep - 1
    r = lax.axis_index("rep")
    v = lax.axis_index("virt")

    a = amplitudes.reshape(rows, per_v // n_rep, n_rep, atom)
    a = jnp.transpose(a, (2, 0, 1, 3)).reshape(n_rep, rows, (per_v // n_rep) * atom)
    masked = jnp.where(cd_irrep[:, None] == ab_irrep[None, :], integrals, jnp.zeros_like(integrals))
    b = masked.reshape(per_k, atom, nb)
    b = jnp.concatenate([b, jnp.zeros((n_rep - per_k, atom, nb), b.dtype)], axis=0)
    b = lax.dynamic_slice_in_dim(jnp.concatenate([b, b], axis=0), r, n_rep, axis=0)
    na = a[0].size
    both = jnp.concatenate([a.reshape(n_rep, -1), b.reshape(n_rep, -1)], axis=1)
    both = lax.all_to_all(both, "rep", split_axis=0, concat_axis=0, tiled=True)
    a = both[:, :na].reshape(n_rep * rows, (per_v // n_rep) * atom)
    b = both[:, na:].reshape(n_rep, atom, nb)

    q = (n_rep - 1 - r) % n_rep
    skip = (jnp.arange(per_k) >= q)[:, None, None]
    b = jnp.where(skip, b[1:], b[:-1])
    b = jnp.broadcast_to(b[None], (n_oy * n_oc,) + b.shape)
    b = lax.all_to_all(b, ("oy", "oc"), split_axis=0, concat_axis=0, tiled=True)
    b = b.reshape(n_virt, -1, nb)
    b = lax.dynamic_slice_in_dim(jnp.concatenate([b, b], axis=0), v, n_virt, axis=0)

    fwd = [(i, (i + 1) % n_virt) for i in range(n_virt)]
    bwd = [(i, (i - 1) % n_virt) for i in range(n_virt)]
    ahead, behind = [], []
    f, g = a, a
    for s in range(1, n_virt // 2 + 1):
        f = lax.ppermute(f, "virt", fwd)
        behind.append(f)
        if s < n_virt - s:
            g = lax.ppermute(g, "virt", bwd)
            ahead.append(g)
    pieces = [a] + ahead + behind[::-1]
    a = jnp.stack(pieces, axis=0)

    partial_sum = jnp.einsum("vmc,vcn->mn", a, b, preferred_element_type=jnp.float32)
    partial_sum = partial_sum.reshape(n_rep, rows, nb)
    partial_sum = lax.all_to_all(partial_sum, "rep", split_axis=0, concat_axis=0, tiled=True)
    return jnp.sum(partial_sum, axis=0)


def solution(mesh):
    n_occ, n_virt, n_rep = mesh.shape["occ"], mesh.shape["virt"], mesh.shape["rep"]
    n_oc = 2 if n_occ % 2 == 0 else 1
    n_oy = n_occ // n_oc
    fine = Mesh(mesh.devices.reshape(n_oy, n_oc, n_virt, n_rep), ("oy", "oc", "virt", "rep"))
    rows_spec = ("oy", "oc", "rep")
    in_specs = (P(rows_spec, "virt"), P(rows_spec, "virt"), P(rows_spec), P("virt"))
    out_specs = P(rows_spec, "virt")

    def body(amplitudes, integrals, cd_irrep, ab_irrep):
        return local(amplitudes, integrals, cd_irrep, ab_irrep, n_rep, n_virt, n_oy, n_oc)

    return jax.shard_map(body, mesh=fine, in_specs=in_specs, out_specs=out_specs, check_vma=False)
```

```python
import math

import jax
import jax.numpy as jnp
from jax import lax
from jax.sharding import Mesh
from jax.sharding import PartitionSpec as P


def local(amplitudes, integrals, cd_irrep, ab_irrep, n_rep, n_virt, n_oy, n_oc):
    rows, cols = amplitudes.shape
    kb, nb = integrals.shape
    atom = math.gcd(cols, kb)
    per_v = cols // atom
    per_k = kb // atom
    assert per_v % n_rep == 0 and per_k == n_rep - 1
    r = lax.axis_index("rep")
    v = lax.axis_index("virt")

    a = amplitudes.reshape(rows, per_v // n_rep, n_rep, atom)
    a = jnp.transpose(a, (2, 0, 1, 3)).reshape(n_rep, rows, (per_v // n_rep) * atom)
    masked = jnp.where(cd_irrep[:, None] == ab_irrep[None, :], integrals, jnp.zeros_like(integrals))
    b = masked.reshape(per_k, atom, nb)
    b = jnp.concatenate([b, jnp.zeros((n_rep - per_k, atom, nb), b.dtype)], axis=0)
    b = lax.dynamic_slice_in_dim(jnp.concatenate([b, b], axis=0), r, n_rep, axis=0)
    na = a[0].size
    both = jnp.concatenate([a.reshape(n_rep, -1), b.reshape(n_rep, -1)], axis=1)
    both = lax.all_to_all(both, "rep", split_axis=0, concat_axis=0, tiled=True)
    a = both[:, :na].reshape(n_rep * rows, (per_v // n_rep) * atom)
    b = both[:, na:].reshape(n_rep, atom, nb)

    q = (n_rep - 1 - r) % n_rep
    skip = (jnp.arange(per_k) >= q)[:, None, None]
    b = jnp.where(skip, b[1:], b[:-1])
    b = jnp.broadcast_to(b[None], (n_oy * n_oc,) + b.shape)
    b = lax.all_to_all(b, ("oy", "oc"), split_axis=0, concat_axis=0, tiled=True)
    b = b.reshape(n_virt, -1, nb)
    b = lax.dynamic_slice_in_dim(jnp.concatenate([b, b], axis=0), v, n_virt, axis=0)

    fwd = [(i, (i + 1) % n_virt) for i in range(n_virt)]
    bwd = [(i, (i - 1) % n_virt) for i in range(n_virt)]
    ahead, behind = [], []
    f, g = a, a
    for s in range(1, n_virt // 2 + 1):
        f = lax.ppermute(f, "virt", fwd)
        behind.append(f)
        if s < n_virt - s:
            g = lax.ppermute(g, "virt", bwd)
            ahead.append(g)
    pieces = lax.optimization_barrier([a] + ahead + behind[::-1])

    partial_sum = sum(jnp.dot(p, b[j], preferred_element_type=jnp.float32) for j, p in enumerate(pieces))
    partial_sum = partial_sum.reshape(n_rep, rows, nb)
    partial_sum = lax.all_to_all(partial_sum, "rep", split_axis=0, concat_axis=0, tiled=True)
    return jnp.sum(partial_sum, axis=0)


def solution(mesh):
    n_occ, n_virt, n_rep = mesh.shape["occ"], mesh.shape["virt"], mesh.shape["rep"]
    n_oc = 2 if n_occ % 2 == 0 else 1
    n_oy = n_occ // n_oc
    fine = Mesh(mesh.devices.reshape(n_oy, n_oc, n_virt, n_rep), ("oy", "oc", "virt", "rep"))
    rows_spec = ("oy", "oc", "rep")
    in_specs = (P(rows_spec, "virt"), P(rows_spec, "virt"), P(rows_spec), P("virt"))
    out_specs = P(rows_spec, "virt")

    def body(amplitudes, integrals, cd_irrep, ab_irrep):
        return local(amplitudes, integrals, cd_irrep, ab_irrep, n_rep, n_virt, n_oy, n_oc)

    return jax.shard_map(body, mesh=fine, in_specs=in_specs, out_specs=out_specs, check_vma=False)
```

```python
import math

import jax
import jax.numpy as jnp
from jax import lax
from jax.sharding import Mesh
from jax.sharding import PartitionSpec as P


def local(amplitudes, integrals, cd_irrep, ab_irrep, n_rep, n_virt, n_oy, n_oc):
    rows, cols = amplitudes.shape
    kb, nb = integrals.shape
    atom = math.gcd(cols, kb)
    per_v = cols // atom
    per_k = kb // atom
    assert per_v % n_rep == 0 and per_k == n_rep - 1
    r = lax.axis_index("rep")
    v = lax.axis_index("virt")

    a = amplitudes.reshape(rows, per_v // n_rep, n_rep, atom)
    a = jnp.transpose(a, (2, 0, 1, 3)).reshape(n_rep, rows, (per_v // n_rep) * atom)
    masked = jnp.where(cd_irrep[:, None] == ab_irrep[None, :], integrals, jnp.zeros_like(integrals))
    b = masked.reshape(per_k, atom, nb)
    b = jnp.concatenate([b, jnp.zeros((n_rep - per_k, atom, nb), b.dtype)], axis=0)
    b = lax.dynamic_slice_in_dim(jnp.concatenate([b, b], axis=0), r, n_rep, axis=0)
    na = a[0].size
    both = jnp.concatenate([a.reshape(n_rep, -1), b.reshape(n_rep, -1)], axis=1)
    both = lax.all_to_all(both, "rep", split_axis=0, concat_axis=0, tiled=True)
    a = both[:, :na].reshape(n_rep * rows, (per_v // n_rep) * atom)
    b = both[:, na:].reshape(n_rep, atom, nb)

    q = (n_rep - 1 - r) % n_rep
    skip = (jnp.arange(per_k) >= q)[:, None, None]
    b = jnp.where(skip, b[1:], b[:-1])
    fwd = [(i, (i + 1) % n_virt) for i in range(n_virt)]
    bwd = [(i, (i - 1) % n_virt) for i in range(n_virt)]
    ahead, behind = [], []
    f, g = a, a
    for s in range(1, n_virt // 2 + 1):
        f = lax.ppermute(f, "virt", fwd)
        if s == 1:
            f, b = lax.optimization_barrier((f, b))
            b = jnp.broadcast_to(b[None], (n_oy * n_oc,) + b.shape)
            b = lax.all_to_all(b, ("oy", "oc"), split_axis=0, concat_axis=0, tiled=True)
            b = b.reshape(n_virt, -1, nb)
            b = lax.dynamic_slice_in_dim(jnp.concatenate([b, b], axis=0), v, n_virt, axis=0)
        behind.append(f)
        if s < n_virt - s:
            g = lax.ppermute(g, "virt", bwd)
            ahead.append(g)
    pieces = [a] + ahead + behind[::-1]
    a = jnp.stack(pieces, axis=0)

    partial_sum = jnp.einsum("vmc,vcn->mn", a, b, preferred_element_type=jnp.float32)
    partial_sum = partial_sum.reshape(n_rep, rows, nb)
    partial_sum = lax.all_to_all(partial_sum, "rep", split_axis=0, concat_axis=0, tiled=True)
    return jnp.sum(partial_sum, axis=0)


def solution(mesh):
    n_occ, n_virt, n_rep = mesh.shape["occ"], mesh.shape["virt"], mesh.shape["rep"]
    n_oc = 2 if n_occ % 2 == 0 else 1
    n_oy = n_occ // n_oc
    fine = Mesh(mesh.devices.reshape(n_oy, n_oc, n_virt, n_rep), ("oy", "oc", "virt", "rep"))
    rows_spec = ("oy", "oc", "rep")
    in_specs = (P(rows_spec, "virt"), P(rows_spec, "virt"), P(rows_spec), P("virt"))
    out_specs = P(rows_spec, "virt")

    def body(amplitudes, integrals, cd_irrep, ab_irrep):
        return local(amplitudes, integrals, cd_irrep, ab_irrep, n_rep, n_virt, n_oy, n_oc)

    return jax.shard_map(body, mesh=fine, in_specs=in_specs, out_specs=out_specs, check_vma=False)
```

```python
import math

import jax
import jax.numpy as jnp
from jax import lax
from jax.sharding import Mesh
from jax.sharding import PartitionSpec as P


def local(amplitudes, integrals, cd_irrep, ab_irrep, n_rep, n_virt, n_oy, n_oc):
    rows, cols = amplitudes.shape
    kb, nb = integrals.shape
    atom = math.gcd(cols, kb)
    per_v = cols // atom
    per_k = kb // atom
    assert per_v % n_rep == 0 and per_k == n_rep - 1
    r = lax.axis_index("rep")
    v = lax.axis_index("virt")

    a = amplitudes.reshape(rows, per_v // n_rep, n_rep, atom)
    a = jnp.transpose(a, (2, 0, 1, 3)).reshape(n_rep, rows, (per_v // n_rep) * atom)
    masked = jnp.where(cd_irrep[:, None] == ab_irrep[None, :], integrals, jnp.zeros_like(integrals))
    b = masked.reshape(per_k, atom, nb)
    b = jnp.concatenate([b, jnp.zeros((n_rep - per_k, atom, nb), b.dtype)], axis=0)
    b = lax.dynamic_slice_in_dim(jnp.concatenate([b, b], axis=0), r, n_rep, axis=0)
    na = a[0].size
    both = jnp.concatenate([a.reshape(n_rep, -1), b.reshape(n_rep, -1)], axis=1)
    both = lax.all_to_all(both, "rep", split_axis=0, concat_axis=0, tiled=True)
    a = both[:, :na].reshape(n_rep * rows, (per_v // n_rep) * atom)
    b = both[:, na:].reshape(n_rep, atom, nb)

    q = (n_rep - 1 - r) % n_rep
    skip = (jnp.arange(per_k) >= q)[:, None, None]
    b = jnp.where(skip, b[1:], b[:-1])
    b = jnp.broadcast_to(b[None], (n_oy * n_oc,) + b.shape)
    b = lax.all_to_all(b, ("oy", "oc"), split_axis=0, concat_axis=0, tiled=True)
    b = b.reshape(n_virt, -1, nb)
    b = lax.dynamic_slice_in_dim(jnp.concatenate([b, b], axis=0), v, n_virt, axis=0)

    fwd = [(i, (i + 1) % n_virt) for i in range(n_virt)]
    bwd = [(i, (i - 1) % n_virt) for i in range(n_virt)]
    stack = jnp.zeros((n_virt,) + a.shape, a.dtype).at[0].set(a)
    f, g = a, a
    for s in range(1, n_virt // 2 + 1):
        f = lax.ppermute(f, "virt", fwd)
        stack = stack.at[n_virt - s].set(f)
        if s < n_virt - s:
            g = lax.ppermute(g, "virt", bwd)
            stack = stack.at[s].set(g)
        stack, f, g = lax.optimization_barrier((stack, f, g))
    a = stack

    partial_sum = jnp.einsum("vmc,vcn->mn", a, b, preferred_element_type=jnp.float32)
    partial_sum = partial_sum.reshape(n_rep, rows, nb)
    partial_sum = lax.all_to_all(partial_sum, "rep", split_axis=0, concat_axis=0, tiled=True)
    return jnp.sum(partial_sum, axis=0)


def solution(mesh):
    n_occ, n_virt, n_rep = mesh.shape["occ"], mesh.shape["virt"], mesh.shape["rep"]
    n_oc = 2 if n_occ % 2 == 0 else 1
    n_oy = n_occ // n_oc
    fine = Mesh(mesh.devices.reshape(n_oy, n_oc, n_virt, n_rep), ("oy", "oc", "virt", "rep"))
    rows_spec = ("oy", "oc", "rep")
    in_specs = (P(rows_spec, "virt"), P(rows_spec, "virt"), P(rows_spec), P("virt"))
    out_specs = P(rows_spec, "virt")

    def body(amplitudes, integrals, cd_irrep, ab_irrep):
        return local(amplitudes, integrals, cd_irrep, ab_irrep, n_rep, n_virt, n_oy, n_oc)

    return jax.shard_map(body, mesh=fine, in_specs=in_specs, out_specs=out_specs, check_vma=False)
```

```python
import math

import jax
import jax.numpy as jnp
from jax import lax
from jax.sharding import Mesh
from jax.sharding import PartitionSpec as P


def local(amplitudes, integrals, cd_irrep, ab_irrep, n_rep, n_virt, n_oy, n_oc):
    rows, cols = amplitudes.shape
    kb, nb = integrals.shape
    atom = math.gcd(cols, kb)
    per_v = cols // atom
    per_k = kb // atom
    assert per_v % n_rep == 0 and per_k == n_rep - 1
    r = lax.axis_index("rep")
    v = lax.axis_index("virt")

    a = amplitudes.reshape(rows, per_v // n_rep, n_rep, atom)
    a = jnp.transpose(a, (2, 0, 1, 3)).reshape(n_rep, rows, (per_v // n_rep) * atom)
    masked = jnp.where(cd_irrep[:, None] == ab_irrep[None, :], integrals, jnp.zeros_like(integrals))
    b = masked.reshape(per_k, atom, nb)
    b = jnp.concatenate([b, jnp.zeros((n_rep - per_k, atom, nb), b.dtype)], axis=0)
    b = lax.dynamic_slice_in_dim(jnp.concatenate([b, b], axis=0), r, n_rep, axis=0)
    na = a[0].size
    both = jnp.concatenate([a.reshape(n_rep, -1), b.reshape(n_rep, -1)], axis=1)
    both = lax.all_to_all(both, "rep", split_axis=0, concat_axis=0, tiled=True)
    a = both[:, :na].reshape(n_rep * rows, (per_v // n_rep) * atom)
    b = both[:, na:].reshape(n_rep, atom, nb)

    q = (n_rep - 1 - r) % n_rep
    skip = (jnp.arange(per_k) >= q)[:, None, None]
    b = jnp.where(skip, b[1:], b[:-1])
    b = jnp.broadcast_to(b[None], (n_oy * n_oc,) + b.shape)
    b = lax.all_to_all(b, ("oy", "oc"), split_axis=0, concat_axis=0, tiled=True)
    b = b.reshape(n_virt, -1, nb)
    b = lax.dynamic_slice_in_dim(jnp.concatenate([b, b], axis=0), v, n_virt, axis=0)

    fwd = [(i, (i + 1) % n_virt) for i in range(n_virt)]
    bwd = [(i, (i - 1) % n_virt) for i in range(n_virt)]
    ahead, behind = [], []
    f, g = a, a
    for s in range(1, n_virt // 2 + 1):
        if s % 2 == 0 and s < n_virt - s:
            g, f = lax.optimization_barrier((lax.ppermute(g, "virt", bwd), f))
            ahead.append(g)
            f = lax.ppermute(f, "virt", fwd)
            behind.append(f)
            continue
        f = lax.ppermute(f, "virt", fwd)
        behind.append(f)
        if s < n_virt - s:
            g = lax.ppermute(g, "virt", bwd)
            ahead.append(g)
    pieces = [a] + ahead + behind[::-1]
    a = jnp.stack(pieces, axis=0)

    partial_sum = jnp.einsum("vmc,vcn->mn", a, b, preferred_element_type=jnp.float32)
    partial_sum = partial_sum.reshape(n_rep, rows, nb)
    partial_sum = lax.all_to_all(partial_sum, "rep", split_axis=0, concat_axis=0, tiled=True)
    return jnp.sum(partial_sum, axis=0)


def solution(mesh):
    n_occ, n_virt, n_rep = mesh.shape["occ"], mesh.shape["virt"], mesh.shape["rep"]
    n_oc = 2 if n_occ % 2 == 0 else 1
    n_oy = n_occ // n_oc
    fine = Mesh(mesh.devices.reshape(n_oy, n_oc, n_virt, n_rep), ("oy", "oc", "virt", "rep"))
    rows_spec = ("oy", "oc", "rep")
    in_specs = (P(rows_spec, "virt"), P(rows_spec, "virt"), P(rows_spec), P("virt"))
    out_specs = P(rows_spec, "virt")

    def body(amplitudes, integrals, cd_irrep, ab_irrep):
        return local(amplitudes, integrals, cd_irrep, ab_irrep, n_rep, n_virt, n_oy, n_oc)

    return jax.shard_map(body, mesh=fine, in_specs=in_specs, out_specs=out_specs, check_vma=False)
```
